512 devices in a mesh: cells: 128 (over y, z, core), dirs: 4 (over x).
Axes of the slice: x: 4, y: 4, z: 16, core: 2. Of those that a mesh axis runs over, the one named last changes fastest.
Arguments:
- incident: float32 [8192, 6144], P('cells', 'dirs'), may hold values from -24 to 24
- scattering: float32 [8192, 192], P('cells'), may hold values from 0.1 to 1
- translations: bfloat16 [8, 192, 192], replicated, may hold values from -1.5 to 1.5
- pair_sphere: int32 [8192, 16], P('cells'), may hold values from 0 to 8191, as said below
- pair_class: int32 [8192, 16], P('cells'), may hold values from 0 to 7
- pair_weight: bfloat16 [8192, 16], P('cells'), may hold values from 0.19921875 to 0.796875
- pair_mask: int32 [8192, 16], P('cells'), may hold values from 0 to 1, as said below
Outputs:
- solution: float32 [8192, 6144], P('cells', 'dirs')
- residual: float32 [8192, 6144], P('cells', 'dirs')
- dual_residual: float32 [8192, 6144], P('cells', 'dirs')
- direction: float32 [8192, 6144], P('cells', 'dirs')
The draws below stay inside these ranges and needn't reach their ends.
Inputs may be any that keep to these rules, and one draw needn't show every extreme that they name: `pair_sphere`: sphere ids are cell-major: cell c holds spheres 64 c to 64 (c + 1) - 1, and the cells form a cycle. The slots of one sphere name distinct spheres, never the sphere itself; each named sphere lies in the sphere's own cell, or among the last 32 spheres of the previous cell, or among the first 32 spheres of the next cell. In every cell the first sphere names sphere 64 - 32 of the previous cell and the last sphere names sphere 32 - 1 of the next, both in live slots. `pair_mask`: the live slots of a sphere come first; the first and the last sphere of every cell have all 16 slots live, every sphere at least 8.
All inputs are finite; a program needn't handle non-finite values.
Results may differ from the reference program's by a relative error of at most 0.0003.
The reference program's roundings to bfloat16 on the way count: a program that leaves them out, or rounds other values in their place, can miss the bound.
Values may be sent and summed in bfloat16 or wider, within the bound.
No kernel may reach another device: no remote copies, remote signals or barrier semaphores. Data moves between devices by JAX's collectives and lax.ppermute only.
A program may use at most 64 MiB of HBM per device.

```python
import math
import jax
import jax.numpy as jnp
from jax import lax

C = 192
DIRS = 32
S_DEV = 64
BAND = 32
NB = 16
CLASSES = 8
SPHERES = 8192


def draw_incident(key, part):
    rows = jnp.arange(SPHERES, dtype=jnp.int32)
    cell_count = SPHERES // S_DEV
    place = (rows // S_DEV).astype(jnp.float32) / jnp.float32(max(cell_count - 1, 1))
    shape = (SPHERES, DIRS * C)
    common_key = jax.random.fold_in(key, 11)
    own_key = jax.random.fold_in(key, 12)
    common = jnp.clip(jax.random.normal(common_key, (1, DIRS * C), jnp.float32), -4.2, 4.2)
    own = jnp.clip(jax.random.normal(own_key, shape, jnp.float32), -4.2, 4.2)
    scale = jnp.float32(4.0) ** place
    values = jnp.float32(0.6) * common + jnp.float32(0.8) * own
    return (values * scale[:, None]).astype(jnp.float32)


def draw_scattering(key, part):
    rows = jnp.arange(SPHERES, dtype=jnp.int32)
    cell_count = SPHERES // S_DEV
    place = (rows // S_DEV).astype(jnp.float32) / jnp.float32(max(cell_count - 1, 1))
    spread = jax.random.uniform(jax.random.fold_in(key, 21), (SPHERES, C), jnp.float32, 0.0, 1.0)
    exponent = jnp.float32(0.7) * place[:, None] + jnp.float32(0.3) * spread
    return (jnp.float32(10.0) ** (-exponent)).astype(jnp.float32)


def draw_translations(key, part):
    noise = jnp.clip(jax.random.normal(jax.random.fold_in(key, 31), (CLASSES, C, C), jnp.float32), -6.0, 6.0)
    noise = noise * jnp.float32(C) ** (-0.5)
    diagonal = jax.random.uniform(jax.random.fold_in(key, 32), (CLASSES, 1, C), jnp.float32, 0.1, 0.3)
    index = jnp.arange(C, dtype=jnp.int32)
    eye = (index[:, None] == index[None, :]).astype(jnp.float32)
    return (noise + eye[None, :, :] * diagonal).astype(jnp.bfloat16)


def draw_pair_sphere(key, part):
    rows = jnp.arange(SPHERES, dtype=jnp.int32)
    within = rows % S_DEV
    owner = rows // S_DEV
    cell_count = SPHERES // S_DEV
    extent = S_DEV + 2 * BAND
    upper_pick = extent // NB - 1
    slots = jnp.arange(NB, dtype=jnp.int32)
    picks = jax.random.randint(key, (SPHERES, NB), 0, upper_pick, dtype=jnp.int32)
    prev_slot = (S_DEV + BAND - 1) % NB
    prev_pick = (S_DEV + BAND - 1) // NB
    next_slot = (BAND - 1) % NB
    next_pick = (BAND - 1) // NB
    picks = jnp.where((within == 0)[:, None] & (slots == prev_slot)[None, :], prev_pick, picks)
    picks = jnp.where((within == S_DEV - 1)[:, None] & (slots == next_slot)[None, :], next_pick, picks)
    spot = (BAND + within[:, None] + 1 + slots[None, :] + NB * picks) % extent
    target_cell = jnp.where(spot < BAND, owner[:, None] - 1, jnp.where(spot < BAND + S_DEV, owner[:, None], owner[:, None] + 1))
    target_cell = target_cell % cell_count
    target_local = jnp.where(spot < BAND, S_DEV - BAND + spot, jnp.where(spot < BAND + S_DEV, spot - BAND, spot - BAND - S_DEV))
    return (target_cell * S_DEV + target_local).astype(jnp.int32)


def draw_pair_mask(key, part):
    rows = jnp.arange(SPHERES, dtype=jnp.int32)
    within = rows % S_DEV
    live = jax.random.randint(key, (SPHERES,), NB // 2, NB + 1, dtype=jnp.int32)
    live = jnp.where((within == 0) | (within == S_DEV - 1), NB, live)
    slots = jnp.arange(NB, dtype=jnp.int32)
    return (slots[None, :] < live[:, None]).astype(jnp.int32)


def set_ends(values, key, least, largest):
    spot = [jax.random.randint(jax.random.fold_in(key, axis), (), 0, length) for axis, length in enumerate(values.shape)]
    widest = values.shape.index(max(values.shape))
    beside = spot[:widest] + [(spot[widest] + 1) % values.shape[widest]] + spot[widest + 1:]
    return values.at[tuple(spot)].set(least).at[tuple(beside)].set(largest)


def block_levels(stream_key, shape, cuts, least, high):
    level = 1.0
    for axis_at, blocks in cuts:
        steps = jax.random.uniform(jax.random.fold_in(jax.random.fold_in(stream_key, 6), axis_at), (blocks,), jnp.float32, least / len(cuts), high / len(cuts))
        level = level * jnp.repeat(jnp.exp(steps), shape[axis_at] // blocks).reshape((-1,) + (1,) * (len(shape) - 1 - axis_at))
    return level


def setup_inputs(seed: int = 0) -> dict:
    key_list = jax.random.split(jax.random.key(seed), 8)
    return {
        "incident": draw_incident(jax.random.fold_in(key_list[7], 71), 0),
        "scattering": draw_scattering(jax.random.fold_in(key_list[7], 71), 0),
        "translations": draw_translations(jax.random.fold_in(key_list[7], 71), 0),
        "pair_sphere": draw_pair_sphere(jax.random.fold_in(key_list[7], 71), 0),
        "pair_class": set_ends(jax.random.randint(key_list[4], (SPHERES, NB), 0, CLASSES), jax.random.fold_in(key_list[4], 1), 0, CLASSES - 1).astype(jnp.int32),
        "pair_weight": jnp.clip(jnp.exp(math.log(0.796875) - 1.3862944 * jax.random.uniform(key_list[5], (SPHERES, NB), jnp.float32) ** block_levels(key_list[5], (SPHERES, NB), ((0, 128),), -0.2, 0.2)), 0.19921875, 0.796875).astype(jnp.bfloat16),
        "pair_mask": draw_pair_mask(jax.random.fold_in(key_list[7], 71), 0),
    }


def reference(incident, scattering, translations, pair_sphere, pair_class, pair_weight, pair_mask):
    cell_count = SPHERES // S_DEV
    columns = incident.shape[1]
    groups = columns // C
    strength = pair_weight.astype(jnp.float32) * pair_mask.astype(jnp.float32)
    source = incident.astype(jnp.bfloat16)
    gain = jnp.tile(scattering, (1, groups))
    sphere_cells = pair_sphere.reshape(cell_count, S_DEV, NB)
    class_cells = pair_class.reshape(cell_count, S_DEV, NB)
    weight_cells = strength.reshape(cell_count, S_DEV, NB)

    def cell_primal(pieces):
        targets, kinds, weights = pieces
        gathered = source[targets].astype(jnp.float32)
        total = jnp.zeros((S_DEV, columns), jnp.float32)
        for klass in range(CLASSES):
            factor = jnp.where(kinds == klass, weights, jnp.float32(0.0))
            summed = jnp.einsum("sm,smd->sd", factor, gathered, precision=lax.Precision.HIGHEST).astype(jnp.bfloat16)
            moved = jnp.dot(summed.reshape(S_DEV * groups, C), translations[klass], preferred_element_type=jnp.float32)
            total = total + moved.reshape(S_DEV, columns)
        return total

    coupled = lax.map(cell_primal, (sphere_cells, class_cells, weight_cells)).reshape(SPHERES, columns)
    image = incident - gain * coupled
    weighted = (gain * incident).astype(jnp.bfloat16)
    weighted_cells = weighted.reshape(cell_count, S_DEV, columns)

    def cell_dual(back, pieces):
        local_rows, targets, kinds, weights = pieces
        moved_all = []
        for klass in range(CLASSES):
            moved = jnp.dot(local_rows.reshape(S_DEV * groups, C), translations[klass].T, preferred_element_type=jnp.float32)
            moved_all.append(moved.reshape(S_DEV, columns))
        stacked = jnp.stack(moved_all, axis=0)
        picks = jnp.where(kinds[:, :, None] == jnp.arange(CLASSES, dtype=jnp.int32)[None, None, :], weights[:, :, None], jnp.float32(0.0))
        contrib = jnp.einsum("smk,ksd->smd", picks, stacked, precision=lax.Precision.HIGHEST)
        back = back.at[targets.reshape(-1)].add(contrib.reshape(S_DEV * NB, columns))
        return back, None

    back, unused = lax.scan(cell_dual, jnp.zeros((SPHERES, columns), jnp.float32), (weighted_cells, sphere_cells, class_cells, weight_cells))
    dual_image = incident - back
    norm_old = jnp.sum(incident * incident)
    curvature = jnp.sum(incident * image)
    step_size = norm_old / curvature
    solution = step_size * incident
    residual = incident - step_size * image
    dual_residual = incident - step_size * dual_image
    norm_new = jnp.sum(residual * dual_residual)
    direction = residual + (norm_new / norm_old) * incident
    return (solution, residual, dual_residual, direction)
```

```python
import jax
import jax.numpy as jnp
from jax import lax
from jax.sharding import PartitionSpec as P


def passed_along(x, axis, by):
    devices = lax.axis_size(axis)
    return lax.ppermute(x, axis, [(i, (i + by) % devices) for i in range(devices)])


def butterfly_sum(v, axes):
    for axis in axes:
        devices = lax.axis_size(axis)
        bit = 1
        while bit < devices:
            v = v + lax.ppermute(v, axis, [(i, i ^ bit) for i in range(devices)])
            bit *= 2
    return v


def on_device(incident, scattering, translations, pair_sphere, pair_class, pair_weight, pair_mask):
    spheres = incident.shape[0]
    columns = incident.shape[1]
    order = translations.shape[1]
    groups = columns // order
    classes = translations.shape[0]
    slots = pair_sphere.shape[1]
    band = spheres // 2
    extent = spheres + 2 * band
    position = lax.axis_index("cells")
    cell_count = lax.axis_size("cells")

    source = incident.astype(jnp.bfloat16)
    from_prev_rows = passed_along(source[spheres - band :], "cells", 1)
    from_next_rows = passed_along(source[:band], "cells", -1)

    owner = pair_sphere // spheres
    within = pair_sphere % spheres
    offset = (owner - position) % cell_count
    column = jnp.where(
        offset == 0,
        band + within,
        jnp.where(offset == 1, band + spheres + within, within - (spheres - band)),
    )
    placed = (column[:, :, None] == jnp.arange(extent, dtype=jnp.int32)[None, None, :]).astype(
        jnp.bfloat16
    )
    strength = pair_weight.astype(jnp.float32) * pair_mask.astype(jnp.float32)
    chosen = pair_class[:, :, None] == jnp.arange(classes, dtype=jnp.int32)[None, None, :]
    coupling = jnp.where(chosen, strength[:, :, None], jnp.float32(0.0)).astype(jnp.bfloat16)
    blocks = jnp.einsum("smk,sme->kse", coupling, placed, preferred_element_type=jnp.float32)
    blocks_half = blocks.astype(jnp.bfloat16)

    gain = jnp.tile(scattering, (1, groups))
    weighted = (gain * incident).astype(jnp.bfloat16).reshape(spheres, groups, order)
    moved = jnp.einsum(
        "sdc,kfc->ksdf", weighted, translations, preferred_element_type=jnp.float32
    ).reshape(classes, spheres, columns)
    contrib = jnp.einsum(
        "kse,ksx->ex",
        blocks,
        moved,
        precision=lax.Precision.HIGHEST,
        preferred_element_type=jnp.float32,
    )
    from_next = passed_along(contrib[:band], "cells", -1)
    from_prev = passed_along(contrib[band + spheres :], "cells", 1)

    padded = jnp.concatenate([from_prev_rows, source, from_next_rows], axis=0)
    gathered = jnp.einsum(
        "kse,ex->ksx", blocks_half, padded, preferred_element_type=jnp.float32
    ).astype(jnp.bfloat16)
    coupled = jnp.einsum(
        "ksdc,kcf->sdf",
        gathered.reshape(classes, spheres, groups, order),
        translations,
        preferred_element_type=jnp.float32,
    ).reshape(spheres, columns)

    back = contrib[band : band + spheres]
    back = back.at[spheres - band :].add(from_next)
    back = back.at[:band].add(from_prev)

    scattered = gain * coupled
    image = incident - scattered
    dual_image = incident - back

    partial = jnp.stack(
        [
            jnp.sum(incident * incident),
            jnp.sum(incident * scattered),
            jnp.sum(incident * back),
            jnp.sum(scattered * back),
        ]
    )
    total = butterfly_sum(partial, ("cells", "dirs"))
    norm_old = total[0]
    cross_u = total[1]
    cross_v = total[2]
    cross_uv = total[3]
    curvature = norm_old - cross_u
    step_size = norm_old / curvature
    keep = -cross_u / curvature
    norm_new = keep * keep * norm_old + keep * step_size * (cross_u + cross_v) + step_size * step_size * cross_uv

    solution = step_size * incident
    residual = incident - step_size * image
    dual_residual = incident - step_size * dual_image
    direction = residual + norm_new / norm_old * incident
    return (solution, residual, dual_residual, direction)


def solution(mesh):
    placed = (
        P("cells", "dirs"),
        P("cells", None),
        P(),
        P("cells", None),
        P("cells", None),
        P("cells", None),
        P("cells", None),
    )
    return jax.shard_map(
        on_device,
        mesh=mesh,
        in_specs=placed,
        out_specs=(P("cells", "dirs"), P("cells", "dirs"), P("cells", "dirs"), P("cells", "dirs")),
        check_vma=False,
    )
```

```python
import jax
import jax.numpy as jnp
from jax import lax
from jax.sharding import PartitionSpec as P


def passed_along(x, axis, by):
    devices = lax.axis_size(axis)
    return lax.ppermute(x, axis, [(i, (i + by) % devices) for i in range(devices)])


def butterfly_sum(v, axes):
    for axis in axes:
        devices = lax.axis_size(axis)
        bit = 1
        while bit < devices:
            v = v + lax.ppermute(v, axis, [(i, i ^ bit) for i in range(devices)])
            bit *= 2
    return v


def on_device(incident, scattering, translations, pair_sphere, pair_class, pair_weight, pair_mask):
    spheres = incident.shape[0]
    columns = incident.shape[1]
    order = translations.shape[1]
    groups = columns // order
    classes = translations.shape[0]
    slots = pair_sphere.shape[1]
    band = spheres // 2
    extent = spheres + 2 * band
    position = lax.axis_index("cells")
    cell_count = lax.axis_size("cells")

    source = incident.astype(jnp.bfloat16)
    from_prev_rows = passed_along(source[spheres - band :], "cells", 1)
    from_next_rows = passed_along(source[:band], "cells", -1)

    owner = pair_sphere // spheres
    within = pair_sphere % spheres
    offset = (owner - position) % cell_count
    column = jnp.where(
        offset == 0,
        band + within,
        jnp.where(offset == 1, band + spheres + within, within - (spheres - band)),
    )
    placed = (column[:, :, None] == jnp.arange(extent, dtype=jnp.int32)[None, None, :]).astype(
        jnp.bfloat16
    )
    strength = pair_weight.astype(jnp.float32) * pair_mask.astype(jnp.float32)
    chosen = pair_class[:, :, None] == jnp.arange(classes, dtype=jnp.int32)[None, None, :]
    coupling = jnp.where(chosen, strength[:, :, None], jnp.float32(0.0)).astype(jnp.bfloat16)
    blocks = jnp.einsum("smk,sme->kse", coupling, placed, preferred_element_type=jnp.float32)
    blocks_half = blocks.astype(jnp.bfloat16)

    gain = jnp.tile(scattering, (1, groups))
    weighted = (gain * incident).astype(jnp.bfloat16).reshape(spheres, groups, order)
    moved = jnp.einsum("sdc,kfc->sdkf", weighted, translations, preferred_element_type=jnp.float32)
    contrib = jnp.einsum(
        "kse,sdkf->edf",
        blocks,
        moved,
        precision=lax.Precision.HIGHEST,
        preferred_element_type=jnp.float32,
    ).reshape(extent, columns)
    from_next = passed_along(contrib[:band], "cells", -1)
    from_prev = passed_along(contrib[band + spheres :], "cells", 1)

    padded = jnp.concatenate([from_prev_rows, source, from_next_rows], axis=0)
    gathered = jnp.einsum(
        "kse,ex->ksx", blocks_half, padded, preferred_element_type=jnp.float32
    ).astype(jnp.bfloat16)
    coupled = jnp.zeros((spheres * groups, order), jnp.float32)
    for klass in range(classes):
        coupled = coupled + jnp.dot(
            gathered[klass].reshape(spheres * groups, order),
            translations[klass],
            preferred_element_type=jnp.float32,
        )
    coupled = coupled.reshape(spheres, columns)

    back = contrib[band : band + spheres]
    back = back.at[spheres - band :].add(from_next)
    back = back.at[:band].add(from_prev)

    scattered = gain * coupled
    image = incident - scattered
    dual_image = incident - back

    partial = jnp.stack(
        [
            jnp.sum(incident * incident),
            jnp.sum(incident * scattered),
            jnp.sum(incident * back),
            jnp.sum(scattered * back),
        ]
    )
    partial = lax.optimization_barrier(partial)
    total = butterfly_sum(partial, ("cells", "dirs"))
    norm_old = total[0]
    cross_u = total[1]
    cross_v = total[2]
    cross_uv = total[3]
    curvature = norm_old - cross_u
    step_size = norm_old / curvature
    keep = -cross_u / curvature
    norm_new = keep * keep * norm_old + keep * step_size * (cross_u + cross_v) + step_size * step_size * cross_uv

    solution = step_size * incident
    residual = incident - step_size * image
    dual_residual = incident - step_size * dual_image
    direction = residual + norm_new / norm_old * incident
    return (solution, residual, dual_residual, direction)


def solution(mesh):
    placed = (
        P("cells", "dirs"),
        P("cells", None),
        P(),
        P("cells", None),
        P("cells", None),
        P("cells", None),
        P("cells", None),
    )
    return jax.shard_map(
        on_device,
        mesh=mesh,
        in_specs=placed,
        out_specs=(P("cells", "dirs"), P("cells", "dirs"), P("cells", "dirs"), P("cells", "dirs")),
        check_vma=False,
    )
```

```python
import jax
import jax.numpy as jnp
from jax import lax
from jax.sharding import Mesh, PartitionSpec as P


def passed_along(x, axes, by):
    devices = 1
    for axis in axes:
        devices *= lax.axis_size(axis)
    return lax.ppermute(x, axes, [(i, (i + by) % devices) for i in range(devices)])


CELLS = ("y", "z", "core")
DIRS = "x"


def exchange_sum(v, axes):
    members = 1
    for axis in axes:
        members *= lax.axis_size(axis)
    spread = jnp.broadcast_to(v[None, :], (members,) + v.shape)
    return jnp.sum(lax.all_to_all(spread, axes, 0, 0, tiled=True), axis=0)


def on_device(incident, scattering, translations, pair_sphere, pair_class, pair_weight, pair_mask):
    spheres = incident.shape[0]
    columns = incident.shape[1]
    order = translations.shape[1]
    groups = columns // order
    classes = translations.shape[0]
    slots = pair_sphere.shape[1]
    band = spheres // 2
    extent = spheres + 2 * band
    position = lax.axis_index(CELLS)
    cell_count = lax.axis_size("y") * lax.axis_size("z") * lax.axis_size("core")

    source = incident.astype(jnp.bfloat16)
    from_prev_rows = passed_along(source[spheres - band :], CELLS, 1)
    from_next_rows = passed_along(source[:band], CELLS, -1)

    owner = pair_sphere // spheres
    within = pair_sphere % spheres
    offset = (owner - position) % cell_count
    column = jnp.where(
        offset == 0,
        band + within,
        jnp.where(offset == 1, band + spheres + within, within - (spheres - band)),
    )
    placed = (column[:, :, None] == jnp.arange(extent, dtype=jnp.int32)[None, None, :]).astype(
        jnp.bfloat16
    )
    strength = pair_weight.astype(jnp.float32) * pair_mask.astype(jnp.float32)
    chosen = pair_class[:, :, None] == jnp.arange(classes, dtype=jnp.int32)[None, None, :]
    coupling = jnp.where(chosen, strength[:, :, None], jnp.float32(0.0)).astype(jnp.bfloat16)
    blocks = jnp.einsum("smk,sme->kse", coupling, placed, preferred_element_type=jnp.float32)
    blocks_half = blocks.astype(jnp.bfloat16)

    gain = jnp.tile(scattering, (1, groups))
    weighted = (gain * incident).astype(jnp.bfloat16).reshape(spheres, groups, order)
    moved = jnp.einsum(
        "sdc,kfc->ksdf", weighted, translations, preferred_element_type=jnp.float32
    ).reshape(classes, spheres, columns)
    contrib = jnp.einsum(
        "kse,ksx->ex",
        blocks,
        moved,
        precision=lax.Precision.HIGHEST,
        preferred_element_type=jnp.float32,
    )
    from_next = passed_along(contrib[:band], CELLS, -1)
    from_prev = passed_along(contrib[band + spheres :], CELLS, 1)

    padded = jnp.concatenate([from_prev_rows, source, from_next_rows], axis=0)
    gathered = jnp.einsum(
        "kse,ex->ksx", blocks_half, padded, preferred_element_type=jnp.float32
    ).astype(jnp.bfloat16)
    coupled = jnp.einsum(
        "ksdc,kcf->sdf",
        gathered.reshape(classes, spheres, groups, order),
        translations,
        preferred_element_type=jnp.float32,
    ).reshape(spheres, columns)

    back = contrib[band : band + spheres]
    back = back.at[spheres - band :].add(from_next)
    back = back.at[:band].add(from_prev)

    scattered = gain * coupled
    image = incident - scattered
    dual_image = incident - back

    partial = jnp.stack(
        [
            jnp.sum(incident * incident),
            jnp.sum(incident * scattered),
            jnp.sum(incident * back),
            jnp.sum(scattered * back),
        ]
    )
    partial = lax.optimization_barrier(partial)
    total = exchange_sum(exchange_sum(partial, ("z", "core")), ("y", DIRS))
    norm_old = total[0]
    cross_u = total[1]
    cross_v = total[2]
    cross_uv = total[3]
    curvature = norm_old - cross_u
    step_size = norm_old / curvature
    keep = -cross_u / curvature
    norm_new = keep * keep * norm_old + keep * step_size * (cross_u + cross_v) + step_size * step_size * cross_uv

    solution = step_size * incident
    residual = incident - step_size * image
    dual_residual = incident - step_size * dual_image
    direction = residual + norm_new / norm_old * incident
    return (solution, residual, dual_residual, direction)


def physical_mesh(mesh):
    devices = mesh.devices
    cores = len({d.core_on_chip for d in devices.flat})
    rows = len({d.coords[1] for d in devices.flat})
    depth = devices.shape[0] // (rows * cores)
    return Mesh(devices.reshape(rows, depth, cores, devices.shape[1]), CELLS + (DIRS,))


def solution(mesh):
    placed = (
        P(CELLS, DIRS),
        P(CELLS, None),
        P(),
        P(CELLS, None),
        P(CELLS, None),
        P(CELLS, None),
        P(CELLS, None),
    )
    return jax.shard_map(
        on_device,
        mesh=physical_mesh(mesh),
        in_specs=placed,
        out_specs=(P(CELLS, DIRS), P(CELLS, DIRS), P(CELLS, DIRS), P(CELLS, DIRS)),
        check_vma=False,
    )
```

```python
import jax
import jax.numpy as jnp
from jax import lax
from jax.sharding import Mesh, PartitionSpec as P


def passed_along(x, axes, by):
    devices = 1
    for axis in axes:
        devices *= lax.axis_size(axis)
    return lax.ppermute(x, axes, [(i, (i + by) % devices) for i in range(devices)])


CELLS = ("y", "z", "core")
DIRS = "x"


def exchange_sum(v, axes):
    members = 1
    for axis in axes:
        members *= lax.axis_size(axis)
    spread = jnp.broadcast_to(v[None, :], (members,) + v.shape)
    return jnp.sum(lax.all_to_all(spread, axes, 0, 0, tiled=True), axis=0)


def on_device(incident, scattering, translations, pair_sphere, pair_class, pair_weight, pair_mask):
    spheres = incident.shape[0]
    columns = incident.shape[1]
    order = translations.shape[1]
    groups = columns // order
    classes = translations.shape[0]
    slots = pair_sphere.shape[1]
    band = spheres // 2
    extent = spheres + 2 * band
    position = lax.axis_index(CELLS)
    cell_count = lax.axis_size("y") * lax.axis_size("z") * lax.axis_size("core")

    source = incident.astype(jnp.bfloat16)

    owner = pair_sphere // spheres
    within = pair_sphere % spheres
    offset = (owner - position) % cell_count
    column = jnp.where(
        offset == 0,
        band + within,
        jnp.where(offset == 1, band + spheres + within, within - (spheres - band)),
    )
    placed = (column[:, :, None] == jnp.arange(extent, dtype=jnp.int32)[None, None, :]).astype(
        jnp.bfloat16
    )
    strength = pair_weight.astype(jnp.float32) * pair_mask.astype(jnp.float32)
    chosen = pair_class[:, :, None] == jnp.arange(classes, dtype=jnp.int32)[None, None, :]
    coupling = jnp.where(chosen, strength[:, :, None], jnp.float32(0.0)).astype(jnp.bfloat16)
    blocks = jnp.einsum("smk,sme->kse", coupling, placed, preferred_element_type=jnp.float32)
    blocks_half = blocks.astype(jnp.bfloat16)

    gain = jnp.tile(scattering, (1, groups))
    weighted = (gain * incident).astype(jnp.bfloat16).reshape(spheres, groups, order)
    moved = jnp.einsum(
        "sdc,kfc->ksdf", weighted, translations, preferred_element_type=jnp.float32
    ).reshape(classes, spheres, columns)
    contrib = jnp.einsum(
        "kse,ksx->ex",
        blocks,
        moved,
        precision=lax.Precision.HIGHEST,
        preferred_element_type=jnp.float32,
    )
    to_next = jnp.concatenate([incident[spheres - band :], contrib[band + spheres :]], axis=0)
    to_prev = jnp.concatenate([incident[:band], contrib[:band]], axis=0)
    from_prev = passed_along(to_next, CELLS, 1)
    from_next = passed_along(to_prev, CELLS, -1)

    own_part = jnp.einsum(
        "kse,ex->ksx", blocks_half[:, :, band : band + spheres], source, preferred_element_type=jnp.float32
    )
    halo = jnp.concatenate([from_prev[:band], from_next[:band]], axis=0).astype(jnp.bfloat16)
    halo_blocks = jnp.concatenate([blocks_half[:, :, :band], blocks_half[:, :, band + spheres :]], axis=2)
    halo_part = jnp.einsum("kse,ex->ksx", halo_blocks, halo, preferred_element_type=jnp.float32)
    gathered = (own_part + halo_part).astype(jnp.bfloat16)
    coupled = jnp.einsum(
        "ksdc,kcf->sdf",
        gathered.reshape(classes, spheres, groups, order),
        translations,
        preferred_element_type=jnp.float32,
    ).reshape(spheres, columns)

    back = contrib[band : band + spheres]
    back = back.at[spheres - band :].add(from_next[band:])
    back = back.at[:band].add(from_prev[band:])

    scattered = gain * coupled
    image = incident - scattered
    dual_image = incident - back

    partial = jnp.stack(
        [
            jnp.sum(incident * incident),
            jnp.sum(incident * scattered),
            jnp.sum(incident * back),
            jnp.sum(scattered * back),
        ]
    )
    partial = lax.optimization_barrier(partial)
    total = exchange_sum(exchange_sum(partial, ("z", "core")), ("y", DIRS))
    rows = lax.optimization_barrier(jnp.broadcast_to(total[:, None], (4, columns)))
    norm_old = rows[0:1]
    cross_u = rows[1:2]
    cross_v = rows[2:3]
    cross_uv = rows[3:4]
    curvature = norm_old - cross_u
    step_size = norm_old / curvature
    keep = -cross_u / curvature
    norm_new = keep * keep * norm_old + keep * step_size * (cross_u + cross_v) + step_size * step_size * cross_uv

    solution = step_size * incident
    residual = incident - step_size * image
    dual_residual = incident - step_size * dual_image
    direction = residual + norm_new / norm_old * incident
    return (solution, residual, dual_residual, direction)


def physical_mesh(mesh):
    devices = mesh.devices
    cores = len({d.core_on_chip for d in devices.flat})
    rows = len({d.coords[1] for d in devices.flat})
    depth = devices.shape[0] // (rows * cores)
    return Mesh(devices.reshape(rows, depth, cores, devices.shape[1]), CELLS + (DIRS,))


def solution(mesh):
    placed = (
        P(CELLS, DIRS),
        P(CELLS, None),
        P(),
        P(CELLS, None),
        P(CELLS, None),
        P(CELLS, None),
        P(CELLS, None),
    )
    return jax.shard_map(
        on_device,
        mesh=physical_mesh(mesh),
        in_specs=placed,
        out_specs=(P(CELLS, DIRS), P(CELLS, DIRS), P(CELLS, DIRS), P(CELLS, DIRS)),
        check_vma=False,
    )
```

```python
import jax
import jax.numpy as jnp
from jax import lax
from jax.sharding import Mesh, PartitionSpec as P


def passed_along(x, axes, by):
    devices = 1
    for axis in axes:
        devices *= lax.axis_size(axis)
    return lax.ppermute(x, axes, [(i, (i + by) % devices) for i in range(devices)])


CELLS = ("y", "z", "core")
DIRS = "x"


def exchange_sum(v, axes):
    members = 1
    for axis in axes:
        members *= lax.axis_size(axis)
    spread = jnp.broadcast_to(v[None, :], (members,) + v.shape)
    return jnp.sum(lax.all_to_all(spread, axes, 0, 0, tiled=True), axis=0)


def on_device(incident, scattering, translations, pair_sphere, pair_class, pair_weight, pair_mask):
    spheres = incident.shape[0]
    columns = incident.shape[1]
    order = translations.shape[1]
    groups = columns // order
    classes = translations.shape[0]
    slots = pair_sphere.shape[1]
    band = spheres // 2
    extent = spheres + 2 * band
    position = lax.axis_index(CELLS)
    cell_count = lax.axis_size("y") * lax.axis_size("z") * lax.axis_size("core")

    source = incident.astype(jnp.bfloat16)
    from_prev_rows = passed_along(source[spheres - band :], CELLS, 1)
    from_next_rows = passed_along(source[:band], CELLS, -1)

    owner = pair_sphere // spheres
    within = pair_sphere % spheres
    offset = (owner - position) % cell_count
    column = jnp.where(
        offset == 0,
        band + within,
        jnp.where(offset == 1, band + spheres + within, within - (spheres - band)),
    )
    placed = (column[:, :, None] == jnp.arange(extent, dtype=jnp.int32)[None, None, :]).astype(
        jnp.bfloat16
    )
    strength = pair_weight.astype(jnp.float32) * pair_mask.astype(jnp.float32)
    chosen = pair_class[:, :, None] == jnp.arange(classes, dtype=jnp.int32)[None, None, :]
    coupling = jnp.where(chosen, strength[:, :, None], jnp.float32(0.0)).astype(jnp.bfloat16)
    blocks = jnp.einsum("smk,sme->kse", coupling, placed, preferred_element_type=jnp.float32)
    blocks_half = blocks.astype(jnp.bfloat16)

    gain = jnp.tile(scattering, (1, groups))
    weighted = (gain * incident).astype(jnp.bfloat16).reshape(spheres, groups, order)
    moved = jnp.einsum(
        "sdc,kfc->ksdf", weighted, translations, preferred_element_type=jnp.float32
    ).reshape(classes, spheres, columns)
    contrib = jnp.einsum(
        "kse,ksx->ex",
        blocks,
        moved,
        precision=lax.Precision.HIGHEST,
        preferred_element_type=jnp.float32,
    )
    from_next = passed_along(contrib[:band], CELLS, -1)
    from_prev = passed_along(contrib[band + spheres :], CELLS, 1)

    padded = jnp.concatenate([from_prev_rows, source, from_next_rows], axis=0)
    gathered = jnp.einsum(
        "kse,ex->ksx", blocks_half, padded, preferred_element_type=jnp.float32
    ).astype(jnp.bfloat16)
    coupled = jnp.einsum(
        "ksdc,kcf->sdf",
        gathered.reshape(classes, spheres, groups, order),
        translations,
        preferred_element_type=jnp.float32,
    ).reshape(spheres, columns)

    back = contrib[band : band + spheres]
    back = back.at[spheres - band :].add(from_next)
    back = back.at[:band].add(from_prev)

    scattered = gain * coupled
    image = incident - scattered
    dual_image = incident - back

    partial = jnp.stack(
        [
            jnp.sum(incident * incident),
            jnp.sum(incident * scattered),
            jnp.sum(incident * back),
            jnp.sum(scattered * back),
        ]
    )
    partial = lax.optimization_barrier(partial)
    total = exchange_sum(exchange_sum(partial, ("z", "core")), ("y", DIRS))
    rows = lax.optimization_barrier(jnp.broadcast_to(total[:, None], (4, columns)))
    norm_old = rows[0:1]
    cross_u = rows[1:2]
    cross_v = rows[2:3]
    cross_uv = rows[3:4]
    curvature = norm_old - cross_u
    step_size = norm_old / curvature
    keep = -cross_u / curvature
    norm_new = keep * keep * norm_old + keep * step_size * (cross_u + cross_v) + step_size * step_size * cross_uv

    solution = step_size * incident
    residual = incident - step_size * image
    dual_residual = incident - step_size * dual_image
    direction = residual + norm_new / norm_old * incident
    return (solution, residual, dual_residual, direction)


def physical_mesh(mesh):
    devices = mesh.devices
    cores = len({d.core_on_chip for d in devices.flat})
    rows = len({d.coords[1] for d in devices.flat})
    depth = devices.shape[0] // (rows * cores)
    return Mesh(devices.reshape(rows, depth, cores, devices.shape[1]), CELLS + (DIRS,))


def solution(mesh):
    placed = (
        P(CELLS, DIRS),
        P(CELLS, None),
        P(),
        P(CELLS, None),
        P(CELLS, None),
        P(CELLS, None),
        P(CELLS, None),
    )
    return jax.shard_map(
        on_device,
        mesh=physical_mesh(mesh),
        in_specs=placed,
        out_specs=(P(CELLS, DIRS), P(CELLS, DIRS), P(CELLS, DIRS), P(CELLS, DIRS)),
        check_vma=False,
    )
```

```python
import jax
import jax.numpy as jnp
from jax import lax
from jax.sharding import Mesh, PartitionSpec as P


def passed_along(x, axes, by):
    devices = 1
    for axis in axes:
        devices *= lax.axis_size(axis)
    return lax.ppermute(x, axes, [(i, (i + by) % devices) for i in range(devices)])


CELLS = ("y", "z", "core")
DIRS = "x"


def exchange_sum(v, axes):
    members = 1
    for axis in axes:
        members *= lax.axis_size(axis)
    spread = jnp.broadcast_to(v[None, :], (members,) + v.shape)
    return jnp.sum(lax.all_to_all(spread, axes, 0, 0, tiled=True), axis=0)


def on_device(incident, scattering, translations, pair_sphere, pair_class, pair_weight, pair_mask):
    spheres = incident.shape[0]
    columns = incident.shape[1]
    order = translations.shape[1]
    groups = columns // order
    classes = translations.shape[0]
    slots = pair_sphere.shape[1]
    band = spheres // 2
    extent = spheres + 2 * band
    position = lax.axis_index(CELLS)
    cell_count = lax.axis_size("y") * lax.axis_size("z") * lax.axis_size("core")

    source = incident.astype(jnp.bfloat16)
    from_prev_rows = passed_along(source[spheres - band :], CELLS, 1)
    from_next_rows = passed_along(source[:band], CELLS, -1)

    owner = pair_sphere // spheres
    within = pair_sphere % spheres
    offset = (owner - position) % cell_count
    column = jnp.where(
        offset == 0,
        band + within,
        jnp.where(offset == 1, band + spheres + within, within - (spheres - band)),
    )
    placed = (column[:, :, None] == jnp.arange(extent, dtype=jnp.int32)[None, None, :]).astype(
        jnp.bfloat16
    )
    strength = pair_weight.astype(jnp.float32) * pair_mask.astype(jnp.float32)
    chosen = pair_class[:, :, None] == jnp.arange(classes, dtype=jnp.int32)[None, None, :]
    coupling = jnp.where(chosen, strength[:, :, None], jnp.float32(0.0)).astype(jnp.bfloat16)
    blocks = jnp.einsum("smk,sme->kse", coupling, placed, preferred_element_type=jnp.float32)
    blocks_half = blocks.astype(jnp.bfloat16)

    gain = jnp.tile(scattering, (1, groups))
    weighted = (gain * incident).astype(jnp.bfloat16).reshape(spheres, groups, order)
    moved = jnp.einsum(
        "sdc,kfc->ksdf", weighted, translations, preferred_element_type=jnp.float32
    ).reshape(classes, spheres, columns)
    contrib = jnp.einsum(
        "kse,ksx->ex",
        blocks,
        moved,
        precision=lax.Precision.HIGHEST,
        preferred_element_type=jnp.float32,
    )
    from_next = passed_along(contrib[:band], CELLS, -1)
    from_prev = passed_along(contrib[band + spheres :], CELLS, 1)

    padded = jnp.concatenate([from_prev_rows, source, from_next_rows], axis=0)
    gathered = jnp.einsum(
        "kse,ex->ksx", blocks_half, padded, preferred_element_type=jnp.float32
    ).astype(jnp.bfloat16)
    coupled = jnp.einsum(
        "ksdc,kcf->sdf",
        gathered.reshape(classes, spheres, groups, order),
        translations,
        preferred_element_type=jnp.float32,
    ).reshape(spheres, columns)

    back = jnp.concatenate(
        [contrib[band : band + band] + from_prev, contrib[band + band : band + spheres] + from_next], axis=0
    )

    scattered = gain * coupled
    image = incident - scattered
    dual_image = incident - back

    partial = jnp.sum(
        jnp.stack([incident * incident, incident * scattered, incident * back, scattered * back]), axis=1
    )
    partial = jnp.sum(lax.optimization_barrier(partial), axis=1)
    partial = lax.optimization_barrier(partial)
    total = exchange_sum(exchange_sum(partial, ("z", "core")), ("y", DIRS))
    rows = lax.optimization_barrier(jnp.broadcast_to(total[:, None], (4, columns)))
    norm_old = rows[0:1]
    cross_u = rows[1:2]
    cross_v = rows[2:3]
    cross_uv = rows[3:4]
    curvature = norm_old - cross_u
    step_size = norm_old / curvature
    keep = -cross_u / curvature
    norm_new = keep * keep * norm_old + keep * step_size * (cross_u + cross_v) + step_size * step_size * cross_uv

    solution = step_size * incident
    residual = incident - step_size * image
    dual_residual = incident - step_size * dual_image
    direction = residual + norm_new / norm_old * incident
    return (solution, residual, dual_residual, direction)


def physical_mesh(mesh):
    devices = mesh.devices
    cores = len({d.core_on_chip for d in devices.flat})
    rows = len({d.coords[1] for d in devices.flat})
    depth = devices.shape[0] // (rows * cores)
    return Mesh(devices.reshape(rows, depth, cores, devices.shape[1]), CELLS + (DIRS,))


def solution(mesh):
    placed = (
        P(CELLS, DIRS),
        P(CELLS, None),
        P(),
        P(CELLS, None),
        P(CELLS, None),
        P(CELLS, None),
        P(CELLS, None),
    )
    return jax.shard_map(
        on_device,
        mesh=physical_mesh(mesh),
        in_specs=placed,
        out_specs=(P(CELLS, DIRS), P(CELLS, DIRS), P(CELLS, DIRS), P(CELLS, DIRS)),
        check_vma=False,
    )
```

```python
import jax
import jax.numpy as jnp
from jax import lax
from jax.sharding import Mesh, PartitionSpec as P


def passed_along(x, axes, by):
    devices = 1
    for axis in axes:
        devices *= lax.axis_size(axis)
    return lax.ppermute(x, axes, [(i, (i + by) % devices) for i in range(devices)])


CELLS = ("y", "z", "core")
DIRS = "x"


def exchange_sum(v, axes):
    members = 1
    for axis in axes:
        members *= lax.axis_size(axis)
    spread = jnp.broadcast_to(v[None, :], (members,) + v.shape)
    return jnp.sum(lax.all_to_all(spread, axes, 0, 0, tiled=True), axis=0)


def on_device(incident, scattering, translations, pair_sphere, pair_class, pair_weight, pair_mask):
    spheres = incident.shape[0]
    columns = incident.shape[1]
    order = translations.shape[1]
    groups = columns // order
    classes = translations.shape[0]
    slots = pair_sphere.shape[1]
    band = spheres // 2
    extent = spheres + 2 * band
    position = lax.axis_index(CELLS)
    cell_count = lax.axis_size("y") * lax.axis_size("z") * lax.axis_size("core")

    source = incident.astype(jnp.bfloat16)
    from_prev_rows = passed_along(source[spheres - band :], CELLS, 1)
    from_next_rows = passed_along(source[:band], CELLS, -1)

    owner = pair_sphere // spheres
    within = pair_sphere % spheres
    offset = (owner - position) % cell_count
    column = jnp.where(
        offset == 0,
        band + within,
        jnp.where(offset == 1, band + spheres + within, within - (spheres - band)),
    )
    placed = (column[:, :, None] == jnp.arange(extent, dtype=jnp.int32)[None, None, :]).astype(
        jnp.bfloat16
    )
    strength = pair_weight.astype(jnp.float32) * pair_mask.astype(jnp.float32)
    chosen = pair_class[:, :, None] == jnp.arange(classes, dtype=jnp.int32)[None, None, :]
    coupling = jnp.where(chosen, strength[:, :, None], jnp.float32(0.0)).astype(jnp.bfloat16)
    blocks = jnp.einsum("smk,sme->kse", coupling, placed, preferred_element_type=jnp.float32)
    blocks_half = blocks.astype(jnp.bfloat16)

    gain = jnp.tile(scattering, (1, groups))
    weighted = (gain * incident).astype(jnp.bfloat16).reshape(spheres, groups, order)
    moved = jnp.einsum(
        "sdc,kfc->ksdf", weighted, translations, preferred_element_type=jnp.float32
    ).reshape(classes, spheres, columns)
    contrib = jnp.einsum(
        "kse,ksx->ex",
        blocks,
        moved,
        precision=lax.Precision.HIGHEST,
        preferred_element_type=jnp.float32,
    )
    from_next = passed_along(contrib[:band], CELLS, -1)
    from_prev = passed_along(contrib[band + spheres :], CELLS, 1)

    padded = jnp.concatenate([from_prev_rows, source, from_next_rows], axis=0)
    padded, blocks_half, unused = lax.optimization_barrier((padded, blocks_half, contrib))
    gathered = jnp.einsum(
        "kse,ex->ksx", blocks_half, padded, preferred_element_type=jnp.float32
    ).astype(jnp.bfloat16)
    coupled = jnp.einsum(
        "ksdc,kcf->sdf",
        gathered.reshape(classes, spheres, groups, order),
        translations,
        preferred_element_type=jnp.float32,
    ).reshape(spheres, columns)

    back = contrib[band : band + spheres]
    back = back.at[spheres - band :].add(from_next)
    back = back.at[:band].add(from_prev)

    scattered = gain * coupled
    image = incident - scattered
    dual_image = incident - back

    partial = jnp.sum(
        jnp.stack([incident * incident, incident * scattered, incident * back, scattered * back]), axis=1
    )
    partial = jnp.sum(lax.optimization_barrier(partial), axis=1)
    partial = lax.optimization_barrier(partial)
    total = exchange_sum(exchange_sum(partial, ("z", "core")), ("y", DIRS))
    rows = lax.optimization_barrier(jnp.broadcast_to(total[:, None], (4, columns)))
    norm_old = rows[0:1]
    cross_u = rows[1:2]
    cross_v = rows[2:3]
    cross_uv = rows[3:4]
    curvature = norm_old - cross_u
    step_size = norm_old / curvature
    keep = -cross_u / curvature
    norm_new = keep * keep * norm_old + keep * step_size * (cross_u + cross_v) + step_size * step_size * cross_uv

    solution = step_size * incident
    residual = incident - step_size * image
    dual_residual = incident - step_size * dual_image
    direction = residual + norm_new / norm_old * incident
    return (solution, residual, dual_residual, direction)


def physical_mesh(mesh):
    devices = mesh.devices
    cores = len({d.core_on_chip for d in devices.flat})
    rows = len({d.coords[1] for d in devices.flat})
    depth = devices.shape[0] // (rows * cores)
    return Mesh(devices.reshape(rows, depth, cores, devices.shape[1]), CELLS + (DIRS,))


def solution(mesh):
    placed = (
        P(CELLS, DIRS),
        P(CELLS, None),
        P(),
        P(CELLS, None),
        P(CELLS, None),
        P(CELLS, None),
        P(CELLS, None),
    )
    return jax.shard_map(
        on_device,
        mesh=physical_mesh(mesh),
        in_specs=placed,
        out_specs=(P(CELLS, DIRS), P(CELLS, DIRS), P(CELLS, DIRS), P(CELLS, DIRS)),
        check_vma=False,
    )
```

```python
import jax
import jax.numpy as jnp
from jax import lax
from jax.sharding import Mesh, PartitionSpec as P


def passed_along(x, axes, by):
    devices = 1
    for axis in axes:
        devices *= lax.axis_size(axis)
    return lax.ppermute(x, axes, [(i, (i + by) % devices) for i in range(devices)])


CELLS = ("y", "z", "core")
DIRS = "x"


def exchange_sum(v, axes):
    members = 1
    for axis in axes:
        members *= lax.axis_size(axis)
    spread = jnp.broadcast_to(v[None, :], (members,) + v.shape)
    return jnp.sum(lax.all_to_all(spread, axes, 0, 0, tiled=True), axis=0)


def on_device(incident, scattering, translations, pair_sphere, pair_class, pair_weight, pair_mask):
    spheres = incident.shape[0]
    columns = incident.shape[1]
    order = translations.shape[1]
    groups = columns // order
    classes = translations.shape[0]
    slots = pair_sphere.shape[1]
    band = spheres // 2
    extent = spheres + 2 * band
    position = lax.axis_index(CELLS)
    cell_count = lax.axis_size("y") * lax.axis_size("z") * lax.axis_size("core")

    source = incident.astype(jnp.bfloat16)

    owner = pair_sphere // spheres
    within = pair_sphere % spheres
    offset = (owner - position) % cell_count
    column = jnp.where(
        offset == 0,
        band + within,
        jnp.where(offset == 1, band + spheres + within, within - (spheres - band)),
    )
    placed = (column[:, :, None] == jnp.arange(extent, dtype=jnp.int32)[None, None, :]).astype(
        jnp.bfloat16
    )
    strength = pair_weight.astype(jnp.float32) * pair_mask.astype(jnp.float32)
    chosen = pair_class[:, :, None] == jnp.arange(classes, dtype=jnp.int32)[None, None, :]
    coupling = jnp.where(chosen, strength[:, :, None], jnp.float32(0.0)).astype(jnp.bfloat16)
    blocks = jnp.einsum("smk,sme->kse", coupling, placed, preferred_element_type=jnp.float32)
    blocks_half = blocks.astype(jnp.bfloat16)

    gain = jnp.tile(scattering, (1, groups))
    weighted = (gain * incident).astype(jnp.bfloat16).reshape(spheres, groups, order)
    moved = jnp.einsum(
        "sdc,kfc->ksdf", weighted, translations, preferred_element_type=jnp.float32
    ).reshape(classes, spheres, columns)
    contrib = jnp.einsum(
        "kse,ksx->ex",
        blocks,
        moved,
        precision=lax.Precision.HIGHEST,
        preferred_element_type=jnp.float32,
    )
    sends = lax.optimization_barrier((source[spheres - band :], source[:band], contrib[:band], contrib[band + spheres :]))
    from_prev_rows = passed_along(sends[0], CELLS, 1)
    from_next_rows = passed_along(sends[1], CELLS, -1)
    from_next = passed_along(sends[2], CELLS, -1)
    from_prev = passed_along(sends[3], CELLS, 1)

    own_part = jnp.einsum(
        "kse,ex->ksx", blocks_half[:, :, band : band + spheres], source, preferred_element_type=jnp.float32
    )
    halo = jnp.concatenate([from_prev_rows, from_next_rows], axis=0)
    halo_blocks = jnp.concatenate([blocks_half[:, :, :band], blocks_half[:, :, band + spheres :]], axis=2)
    halo_part = jnp.einsum("kse,ex->ksx", halo_blocks, halo, preferred_element_type=jnp.float32)
    gathered = (own_part + halo_part).astype(jnp.bfloat16)
    coupled = jnp.einsum(
        "ksdc,kcf->sdf",
        gathered.reshape(classes, spheres, groups, order),
        translations,
        preferred_element_type=jnp.float32,
    ).reshape(spheres, columns)

    back = contrib[band : band + spheres]
    back = back.at[spheres - band :].add(from_next)
    back = back.at[:band].add(from_prev)

    scattered = gain * coupled
    image = incident - scattered
    dual_image = incident - back

    partial = jnp.sum(
        jnp.stack([incident * incident, incident * scattered, incident * back, scattered * back]), axis=1
    )
    partial = jnp.sum(lax.optimization_barrier(partial), axis=1)
    partial = lax.optimization_barrier(partial)
    total = exchange_sum(exchange_sum(partial, ("z", "core")), ("y", DIRS))
    rows = lax.optimization_barrier(jnp.broadcast_to(total[:, None], (4, columns)))
    norm_old = rows[0:1]
    cross_u = rows[1:2]
    cross_v = rows[2:3]
    cross_uv = rows[3:4]
    curvature = norm_old - cross_u
    step_size = norm_old / curvature
    keep = -cross_u / curvature
    norm_new = keep * keep * norm_old + keep * step_size * (cross_u + cross_v) + step_size * step_size * cross_uv

    solution = step_size * incident
    residual = incident - step_size * image
    dual_residual = incident - step_size * dual_image
    direction = residual + norm_new / norm_old * incident
    return (solution, residual, dual_residual, direction)


def physical_mesh(mesh):
    devices = mesh.devices
    cores = len({d.core_on_chip for d in devices.flat})
    rows = len({d.coords[1] for d in devices.flat})
    depth = devices.shape[0] // (rows * cores)
    return Mesh(devices.reshape(rows, depth, cores, devices.shape[1]), CELLS + (DIRS,))


def solution(mesh):
    placed = (
        P(CELLS, DIRS),
        P(CELLS, None),
        P(),
        P(CELLS, None),
        P(CELLS, None),
        P(CELLS, None),
        P(CELLS, None),
    )
    return jax.shard_map(
        on_device,
        mesh=physical_mesh(mesh),
        in_specs=placed,
        out_specs=(P(CELLS, DIRS), P(CELLS, DIRS), P(CELLS, DIRS), P(CELLS, DIRS)),
        check_vma=False,
    )
```

```python
import jax
import jax.numpy as jnp
from jax import lax
from jax.sharding import Mesh, PartitionSpec as P


def passed_along(x, axes, by):
    devices = 1
    for axis in axes:
        devices *= lax.axis_size(axis)
    return lax.ppermute(x, axes, [(i, (i + by) % devices) for i in range(devices)])


CELLS = ("y", "z", "core")
DIRS = "x"


def exchange_sum(v, axes):
    members = 1
    for axis in axes:
        members *= lax.axis_size(axis)
    spread = jnp.broadcast_to(v[None, :], (members,) + v.shape)
    return jnp.sum(lax.all_to_all(spread, axes, 0, 0, tiled=True), axis=0)


def on_device(incident, scattering, translations, pair_sphere, pair_class, pair_weight, pair_mask):
    spheres = incident.shape[0]
    columns = incident.shape[1]
    order = translations.shape[1]
    groups = columns // order
    classes = translations.shape[0]
    slots = pair_sphere.shape[1]
    band = spheres // 2
    extent = spheres + 2 * band
    position = lax.axis_index(CELLS)
    cell_count = lax.axis_size("y") * lax.axis_size("z") * lax.axis_size("core")

    source = incident.astype(jnp.bfloat16)

    owner = pair_sphere // spheres
    within = pair_sphere % spheres
    offset = (owner - position) % cell_count
    column = jnp.where(
        offset == 0,
        band + within,
        jnp.where(offset == 1, band + spheres + within, within - (spheres - band)),
    )
    placed = (column[:, :, None] == jnp.arange(extent, dtype=jnp.int32)[None, None, :]).astype(
        jnp.bfloat16
    )
    strength = pair_weight.astype(jnp.float32) * pair_mask.astype(jnp.float32)
    chosen = pair_class[:, :, None] == jnp.arange(classes, dtype=jnp.int32)[None, None, :]
    coupling = jnp.where(chosen, strength[:, :, None], jnp.float32(0.0)).astype(jnp.bfloat16)
    blocks = jnp.einsum("smk,sme->kse", coupling, placed, preferred_element_type=jnp.float32)
    blocks_half = blocks.astype(jnp.bfloat16)

    gain = jnp.tile(scattering, (1, groups))
    weighted = (gain * incident).astype(jnp.bfloat16).reshape(spheres, groups, order)
    moved = jnp.einsum(
        "sdc,kfc->ksdf", weighted, translations, preferred_element_type=jnp.float32
    ).reshape(classes, spheres, columns)
    high = lax.reduce_precision(moved, exponent_bits=8, mantissa_bits=7)
    rest = moved - high
    middle = lax.reduce_precision(rest, exponent_bits=8, mantissa_bits=7)
    low = rest - middle
    pieces = jnp.concatenate(
        [high.astype(jnp.bfloat16), middle.astype(jnp.bfloat16), low.astype(jnp.bfloat16)], axis=0
    )
    contrib = jnp.einsum(
        "kse,ksx->ex",
        jnp.concatenate([blocks_half] * 3, axis=0),
        pieces,
        preferred_element_type=jnp.float32,
    )
    sends = lax.optimization_barrier((source[spheres - band :], source[:band], contrib[:band], contrib[band + spheres :]))
    from_prev_rows = passed_along(sends[0], CELLS, 1)
    from_next_rows = passed_along(sends[1], CELLS, -1)
    from_next = passed_along(sends[2], CELLS, -1)
    from_prev = passed_along(sends[3], CELLS, 1)

    own_part = jnp.einsum(
        "kse,ex->ksx", blocks_half[:, :, band : band + spheres], source, preferred_element_type=jnp.float32
    )
    halo = jnp.concatenate([from_prev_rows, from_next_rows], axis=0)
    halo_blocks = jnp.concatenate([blocks_half[:, :, :band], blocks_half[:, :, band + spheres :]], axis=2)
    halo_part = jnp.einsum("kse,ex->ksx", halo_blocks, halo, preferred_element_type=jnp.float32)
    gathered = (own_part + halo_part).astype(jnp.bfloat16)
    coupled = jnp.einsum(
        "ksdc,kcf->sdf",
        gathered.reshape(classes, spheres, groups, order),
        translations,
        preferred_element_type=jnp.float32,
    ).reshape(spheres, columns)

    back = contrib[band : band + spheres]
    back = back.at[spheres - band :].add(from_next)
    back = back.at[:band].add(from_prev)

    scattered = gain * coupled
    image = incident - scattered
    dual_image = incident - back

    partial = jnp.sum(
        jnp.stack([incident * incident, incident * scattered, incident * back, scattered * back]), axis=1
    )
    partial = jnp.sum(lax.optimization_barrier(partial), axis=1)
    partial = lax.optimization_barrier(partial)
    total = exchange_sum(exchange_sum(partial, ("z", "core")), ("y", DIRS))
    rows = lax.optimization_barrier(jnp.broadcast_to(total[:, None], (4, columns)))
    norm_old = rows[0:1]
    cross_u = rows[1:2]
    cross_v = rows[2:3]
    cross_uv = rows[3:4]
    curvature = norm_old - cross_u
    step_size = norm_old / curvature
    keep = -cross_u / curvature
    norm_new = keep * keep * norm_old + keep * step_size * (cross_u + cross_v) + step_size * step_size * cross_uv

    solution = step_size * incident
    residual = incident - step_size * image
    dual_residual = incident - step_size * dual_image
    direction = residual + norm_new / norm_old * incident
    return (solution, residual, dual_residual, direction)


def physical_mesh(mesh):
    devices = mesh.devices
    cores = len({d.core_on_chip for d in devices.flat})
    rows = len({d.coords[1] for d in devices.flat})
    depth = devices.shape[0] // (rows * cores)
    return Mesh(devices.reshape(rows, depth, cores, devices.shape[1]), CELLS + (DIRS,))


def solution(mesh):
    placed = (
        P(CELLS, DIRS),
        P(CELLS, None),
        P(),
        P(CELLS, None),
        P(CELLS, None),
        P(CELLS, None),
        P(CELLS, None),
    )
    return jax.shard_map(
        on_device,
        mesh=physical_mesh(mesh),
        in_specs=placed,
        out_specs=(P(CELLS, DIRS), P(CELLS, DIRS), P(CELLS, DIRS), P(CELLS, DIRS)),
        check_vma=False,
    )
```

```python
import jax
import jax.numpy as jnp
from jax import lax
from jax.sharding import Mesh, PartitionSpec as P


def passed_along(x, axes, by):
    devices = 1
    for axis in axes:
        devices *= lax.axis_size(axis)
    return lax.ppermute(x, axes, [(i, (i + by) % devices) for i in range(devices)])


CELLS = ("y", "z", "core")
DIRS = "x"


def exchange_sum(v, axes):
    members = 1
    for axis in axes:
        members *= lax.axis_size(axis)
    spread = jnp.broadcast_to(v[None, :], (members,) + v.shape)
    return jnp.sum(lax.all_to_all(spread, axes, 0, 0, tiled=True), axis=0)


def on_device(incident, scattering, translations, pair_sphere, pair_class, pair_weight, pair_mask):
    spheres = incident.shape[0]
    columns = incident.shape[1]
    order = translations.shape[1]
    groups = columns // order
    classes = translations.shape[0]
    slots = pair_sphere.shape[1]
    band = spheres // 2
    extent = spheres + 2 * band
    position = lax.axis_index(CELLS)
    cell_count = lax.axis_size("y") * lax.axis_size("z") * lax.axis_size("core")

    source = incident.astype(jnp.bfloat16)
    from_prev_rows = passed_along(source[spheres - band :], CELLS, 1)
    from_next_rows = passed_along(source[:band], CELLS, -1)

    owner = pair_sphere // spheres
    within = pair_sphere % spheres
    offset = (owner - position) % cell_count
    column = jnp.where(
        offset == 0,
        band + within,
        jnp.where(offset == 1, band + spheres + within, within - (spheres - band)),
    )
    strength = pair_weight.astype(jnp.float32) * pair_mask.astype(jnp.float32)
    hit = (pair_class[:, :, None, None] == jnp.arange(classes, dtype=jnp.int32)[None, None, :, None]) & (
        column[:, :, None, None] == jnp.arange(extent, dtype=jnp.int32)[None, None, None, :]
    )
    blocks = jnp.sum(jnp.where(hit, strength[:, :, None, None], jnp.float32(0.0)), axis=1).transpose(1, 0, 2)
    blocks_half = blocks.astype(jnp.bfloat16)

    gain = jnp.tile(scattering, (1, groups))
    weighted = (gain * incident).astype(jnp.bfloat16).reshape(spheres, groups, order)
    moved = jnp.einsum(
        "sdc,kfc->ksdf", weighted, translations, preferred_element_type=jnp.float32
    ).reshape(classes, spheres, columns)
    contrib = jnp.einsum(
        "kse,ksx->ex",
        blocks,
        moved,
        precision=lax.Precision.HIGHEST,
        preferred_element_type=jnp.float32,
    )
    from_next = passed_along(contrib[:band], CELLS, -1)
    from_prev = passed_along(contrib[band + spheres :], CELLS, 1)

    padded = jnp.concatenate([from_prev_rows, source, from_next_rows], axis=0)
    padded, blocks_half, unused = lax.optimization_barrier((padded, blocks_half, contrib))
    gathered = jnp.einsum(
        "kse,ex->ksx", blocks_half, padded, preferred_element_type=jnp.float32
    ).astype(jnp.bfloat16)
    coupled = jnp.einsum(
        "ksdc,kcf->sdf",
        gathered.reshape(classes, spheres, groups, order),
        translations,
        preferred_element_type=jnp.float32,
    ).reshape(spheres, columns)

    back = contrib[band : band + spheres]
    back = back.at[spheres - band :].add(from_next)
    back = back.at[:band].add(from_prev)

    scattered = gain * coupled
    image = incident - scattered
    dual_image = incident - back

    partial = jnp.sum(
        jnp.stack([incident * incident, incident * scattered, incident * back, scattered * back]), axis=1
    )
    partial = jnp.sum(lax.optimization_barrier(partial), axis=1)
    partial = lax.optimization_barrier(partial)
    total = exchange_sum(exchange_sum(partial, ("z", "core")), ("y", DIRS))
    rows = lax.optimization_barrier(jnp.broadcast_to(total[:, None], (4, columns)))
    norm_old = rows[0:1]
    cross_u = rows[1:2]
    cross_v = rows[2:3]
    cross_uv = rows[3:4]
    curvature = norm_old - cross_u
    step_size = norm_old / curvature
    keep = -cross_u / curvature
    norm_new = keep * keep * norm_old + keep * step_size * (cross_u + cross_v) + step_size * step_size * cross_uv

    solution = step_size * incident
    residual = incident - step_size * image
    dual_residual = incident - step_size * dual_image
    direction = residual + norm_new / norm_old * incident
    return (solution, residual, dual_residual, direction)


def physical_mesh(mesh):
    devices = mesh.devices
    cores = len({d.core_on_chip for d in devices.flat})
    rows = len({d.coords[1] for d in devices.flat})
    depth = devices.shape[0] // (rows * cores)
    return Mesh(devices.reshape(rows, depth, cores, devices.shape[1]), CELLS + (DIRS,))


def solution(mesh):
    placed = (
        P(CELLS, DIRS),
        P(CELLS, None),
        P(),
        P(CELLS, None),
        P(CELLS, None),
        P(CELLS, None),
        P(CELLS, None),
    )
    return jax.shard_map(
        on_device,
        mesh=physical_mesh(mesh),
        in_specs=placed,
        out_specs=(P(CELLS, DIRS), P(CELLS, DIRS), P(CELLS, DIRS), P(CELLS, DIRS)),
        check_vma=False,
    )
```

```python
import jax
import jax.numpy as jnp
from jax import lax
from jax.sharding import Mesh, PartitionSpec as P


def passed_along(x, axes, by):
    devices = 1
    for axis in axes:
        devices *= lax.axis_size(axis)
    return lax.ppermute(x, axes, [(i, (i + by) % devices) for i in range(devices)])


CELLS = ("y", "z", "core")
DIRS = "x"


def exchange_sum(v, axes):
    members = 1
    for axis in axes:
        members *= lax.axis_size(axis)
    spread = jnp.broadcast_to(v[None, :], (members,) + v.shape)
    return jnp.sum(lax.all_to_all(spread, axes, 0, 0, tiled=True), axis=0)


def on_device(incident, scattering, translations, pair_sphere, pair_class, pair_weight, pair_mask):
    spheres = incident.shape[0]
    columns = incident.shape[1]
    order = translations.shape[1]
    groups = columns // order
    classes = translations.shape[0]
    slots = pair_sphere.shape[1]
    band = spheres // 2
    extent = spheres + 2 * band
    position = lax.axis_index(CELLS)
    cell_count = lax.axis_size("y") * lax.axis_size("z") * lax.axis_size("core")

    source = incident.astype(jnp.bfloat16)
    from_prev_rows = passed_along(source[spheres - band :], CELLS, 1)
    from_next_rows = passed_along(source[:band], CELLS, -1)

    owner = pair_sphere // spheres
    within = pair_sphere % spheres
    offset = (owner - position) % cell_count
    column = jnp.where(
        offset == 0,
        band + within,
        jnp.where(offset == 1, band + spheres + within, within - (spheres - band)),
    )
    placed = (column[:, :, None] == jnp.arange(extent, dtype=jnp.int32)[None, None, :]).astype(
        jnp.bfloat16
    )
    strength = pair_weight.astype(jnp.float32) * pair_mask.astype(jnp.float32)
    chosen = pair_class[:, :, None] == jnp.arange(classes, dtype=jnp.int32)[None, None, :]
    coupling = jnp.where(chosen, strength[:, :, None], jnp.float32(0.0)).astype(jnp.bfloat16)
    blocks = jnp.einsum("smk,sme->kse", coupling, placed, preferred_element_type=jnp.float32)
    blocks_half = blocks.astype(jnp.bfloat16)

    gain = jnp.tile(scattering, (1, groups))
    weighted = (gain * incident).astype(jnp.bfloat16).reshape(spheres, groups, order)
    moved = jnp.einsum(
        "sdc,kfc->ksdf", weighted, translations, preferred_element_type=jnp.float32
    ).reshape(classes, spheres, columns)
    contrib = jnp.einsum(
        "kse,ksx->ex",
        blocks,
        moved,
        precision=lax.Precision.HIGHEST,
        preferred_element_type=jnp.float32,
    )
    sends = lax.optimization_barrier((contrib[:band], contrib[band + spheres :]))
    from_next = passed_along(sends[0], CELLS, -1)
    from_prev = passed_along(sends[1], CELLS, 1)

    padded = jnp.concatenate([from_prev_rows, source, from_next_rows], axis=0)
    padded, blocks_half, unused = lax.optimization_barrier((padded, blocks_half, contrib))
    gathered = jnp.einsum(
        "kse,ex->ksx", blocks_half, padded, preferred_element_type=jnp.float32
    ).astype(jnp.bfloat16)
    coupled = jnp.einsum(
        "ksdc,kcf->sdf",
        gathered.reshape(classes, spheres, groups, order),
        translations,
        preferred_element_type=jnp.float32,
    ).reshape(spheres, columns)

    back = jnp.concatenate(
        [contrib[band : band + band] + from_prev, contrib[band + band : band + spheres] + from_next], axis=0
    )

    scattered = gain * coupled
    image = incident - scattered
    dual_image = incident - back

    partial = jnp.sum(
        jnp.stack([incident * incident, incident * scattered, incident * back, scattered * back]), axis=1
    )
    partial = jnp.sum(lax.optimization_barrier(partial), axis=1)
    partial = lax.optimization_barrier(partial)
    total = exchange_sum(exchange_sum(partial, ("z", "core")), ("y", DIRS))
    rows = lax.optimization_barrier(jnp.broadcast_to(total[:, None], (4, columns)))
    norm_old = rows[0:1]
    cross_u = rows[1:2]
    cross_v = rows[2:3]
    cross_uv = rows[3:4]
    curvature = norm_old - cross_u
    step_size = norm_old / curvature
    keep = -cross_u / curvature
    norm_new = keep * keep * norm_old + keep * step_size * (cross_u + cross_v) + step_size * step_size * cross_uv

    solution = step_size * incident
    residual = incident - step_size * image
    dual_residual = incident - step_size * dual_image
    direction = residual + norm_new / norm_old * incident
    return (solution, residual, dual_residual, direction)


def physical_mesh(mesh):
    devices = mesh.devices
    cores = len({d.core_on_chip for d in devices.flat})
    rows = len({d.coords[1] for d in devices.flat})
    depth = devices.shape[0] // (rows * cores)
    return Mesh(devices.reshape(rows, depth, cores, devices.shape[1]), CELLS + (DIRS,))


def solution(mesh):
    placed = (
        P(CELLS, DIRS),
        P(CELLS, None),
        P(),
        P(CELLS, None),
        P(CELLS, None),
        P(CELLS, None),
        P(CELLS, None),
    )
    return jax.shard_map(
        on_device,
        mesh=physical_mesh(mesh),
        in_specs=placed,
        out_specs=(P(CELLS, DIRS), P(CELLS, DIRS), P(CELLS, DIRS), P(CELLS, DIRS)),
        check_vma=False,
    )
```

```python
import jax
import jax.numpy as jnp
from jax import lax
from jax.sharding import Mesh, PartitionSpec as P


def passed_along(x, axes, by):
    devices = 1
    for axis in axes:
        devices *= lax.axis_size(axis)
    return lax.ppermute(x, axes, [(i, (i + by) % devices) for i in range(devices)])


CELLS = ("y", "z", "core")
DIRS = "x"


def exchange_sum(v, axes):
    members = 1
    for axis in axes:
        members *= lax.axis_size(axis)
    spread = jnp.broadcast_to(v[None, :], (members,) + v.shape)
    return jnp.sum(lax.all_to_all(spread, axes, 0, 0, tiled=True), axis=0)


def on_device(incident, scattering, translations, pair_sphere, pair_class, pair_weight, pair_mask):
    spheres = incident.shape[0]
    columns = incident.shape[1]
    order = translations.shape[1]
    groups = columns // order
    classes = translations.shape[0]
    slots = pair_sphere.shape[1]
    band = spheres // 2
    extent = spheres + 2 * band
    position = lax.axis_index(CELLS)
    cell_count = lax.axis_size("y") * lax.axis_size("z") * lax.axis_size("core")

    source = incident.astype(jnp.bfloat16)
    from_prev_rows = passed_along(source[spheres - band :], CELLS, 1)
    from_next_rows = passed_along(source[:band], CELLS, -1)

    owner = pair_sphere // spheres
    within = pair_sphere % spheres
    offset = (owner - position) % cell_count
    column = jnp.where(
        offset == 0,
        band + within,
        jnp.where(offset == 1, band + spheres + within, within - (spheres - band)),
    )
    placed = (column[:, :, None] == jnp.arange(extent, dtype=jnp.int32)[None, None, :]).astype(
        jnp.bfloat16
    )
    strength = pair_weight.astype(jnp.float32) * pair_mask.astype(jnp.float32)
    chosen = pair_class[:, :, None] == jnp.arange(classes, dtype=jnp.int32)[None, None, :]
    coupling = jnp.where(chosen, strength[:, :, None], jnp.float32(0.0)).astype(jnp.bfloat16)
    blocks = jnp.einsum("smk,sme->kse", coupling, placed, preferred_element_type=jnp.float32)
    blocks_half = blocks.astype(jnp.bfloat16)

    gain = jnp.tile(scattering, (1, groups))
    weighted = (gain * incident).astype(jnp.bfloat16).reshape(spheres, groups, order)
    moved = jnp.einsum(
        "sdc,kfc->ksdf", weighted, translations, preferred_element_type=jnp.float32
    ).reshape(classes, spheres, columns)
    contrib = jnp.einsum(
        "kse,ksx->ex",
        blocks,
        moved,
        precision=lax.Precision.HIGH,
        preferred_element_type=jnp.float32,
    )
    sends = lax.optimization_barrier((contrib[:band], contrib[band + spheres :]))
    from_next = passed_along(sends[0], CELLS, -1)
    from_prev = passed_along(sends[1], CELLS, 1)

    padded = jnp.concatenate([from_prev_rows, source, from_next_rows], axis=0)
    padded, blocks_half, unused = lax.optimization_barrier((padded, blocks_half, contrib))
    gathered = jnp.einsum(
        "kse,ex->ksx", blocks_half, padded, preferred_element_type=jnp.float32
    ).astype(jnp.bfloat16)
    coupled = jnp.einsum(
        "ksdc,kcf->sdf",
        gathered.reshape(classes, spheres, groups, order),
        translations,
        preferred_element_type=jnp.float32,
    ).reshape(spheres, columns)

    back = jnp.concatenate(
        [contrib[band : band + band] + from_prev, contrib[band + band : band + spheres] + from_next], axis=0
    )

    scattered = gain * coupled
    image = incident - scattered
    dual_image = incident - back

    partial = jnp.sum(
        jnp.stack([incident * incident, incident * scattered, incident * back, scattered * back]), axis=1
    )
    partial = jnp.sum(lax.optimization_barrier(partial), axis=1)
    partial = lax.optimization_barrier(partial)
    total = exchange_sum(exchange_sum(partial, ("z", "core")), ("y", DIRS))
    rows = lax.optimization_barrier(jnp.broadcast_to(total[:, None], (4, columns)))
    norm_old = rows[0:1]
    cross_u = rows[1:2]
    cross_v = rows[2:3]
    cross_uv = rows[3:4]
    curvature = norm_old - cross_u
    step_size = norm_old / curvature
    keep = -cross_u / curvature
    norm_new = keep * keep * norm_old + keep * step_size * (cross_u + cross_v) + step_size * step_size * cross_uv

    solution = step_size * incident
    residual = incident - step_size * image
    dual_residual = incident - step_size * dual_image
    direction = residual + norm_new / norm_old * incident
    return (solution, residual, dual_residual, direction)


def physical_mesh(mesh):
    devices = mesh.devices
    cores = len({d.core_on_chip for d in devices.flat})
    rows = len({d.coords[1] for d in devices.flat})
    depth = devices.shape[0] // (rows * cores)
    return Mesh(devices.reshape(rows, depth, cores, devices.shape[1]), CELLS + (DIRS,))


def solution(mesh):
    placed = (
        P(CELLS, DIRS),
        P(CELLS, None),
        P(),
        P(CELLS, None),
        P(CELLS, None),
        P(CELLS, None),
        P(CELLS, None),
    )
    return jax.shard_map(
        on_device,
        mesh=physical_mesh(mesh),
        in_specs=placed,
        out_specs=(P(CELLS, DIRS), P(CELLS, DIRS), P(CELLS, DIRS), P(CELLS, DIRS)),
        check_vma=False,
    )
```

```python
import jax
import jax.numpy as jnp
from jax import lax
from jax.sharding import Mesh, PartitionSpec as P


def passed_along(x, axes, by):
    devices = 1
    for axis in axes:
        devices *= lax.axis_size(axis)
    return lax.ppermute(x, axes, [(i, (i + by) % devices) for i in range(devices)])


CELLS = ("y", "z", "core")
DIRS = "x"


def exchange_sum(v, axes):
    members = 1
    for axis in axes:
        members *= lax.axis_size(axis)
    spread = jnp.broadcast_to(v[None, :], (members,) + v.shape)
    return jnp.sum(lax.all_to_all(spread, axes, 0, 0, tiled=True), axis=0)


def on_device(incident, scattering, translations, pair_sphere, pair_class, pair_weight, pair_mask):
    spheres = incident.shape[0]
    columns = incident.shape[1]
    order = translations.shape[1]
    groups = columns // order
    classes = translations.shape[0]
    slots = pair_sphere.shape[1]
    band = spheres // 2
    extent = spheres + 2 * band
    position = lax.axis_index(CELLS)
    cell_count = lax.axis_size("y") * lax.axis_size("z") * lax.axis_size("core")

    source = incident.astype(jnp.bfloat16)
    from_prev_rows = passed_along(source[spheres - band :], CELLS, 1)
    from_next_rows = passed_along(source[:band], CELLS, -1)

    owner = pair_sphere // spheres
    within = pair_sphere % spheres
    offset = (owner - position) % cell_count
    column = jnp.where(
        offset == 0,
        band + within,
        jnp.where(offset == 1, band + spheres + within, within - (spheres - band)),
    )
    placed = (column[:, :, None] == jnp.arange(extent, dtype=jnp.int32)[None, None, :]).astype(
        jnp.bfloat16
    )
    strength = pair_weight.astype(jnp.float32) * pair_mask.astype(jnp.float32)
    chosen = pair_class[:, :, None] == jnp.arange(classes, dtype=jnp.int32)[None, None, :]
    coupling = jnp.where(chosen, strength[:, :, None], jnp.float32(0.0)).astype(jnp.bfloat16)
    blocks = jnp.einsum("smk,sme->kse", coupling, placed, preferred_element_type=jnp.float32)
    blocks_half = blocks.astype(jnp.bfloat16)

    gain = jnp.tile(scattering, (1, groups))
    weighted = (gain * incident).astype(jnp.bfloat16).reshape(spheres, groups, order)
    moved = jnp.einsum(
        "sdc,kfc->ksdf", weighted, translations, preferred_element_type=jnp.float32
    ).reshape(classes, spheres, columns)
    contrib = jnp.einsum(
        "kse,ksx->ex",
        blocks,
        moved,
        precision=lax.Precision.HIGH,
        preferred_element_type=jnp.float32,
    )
    sends = lax.optimization_barrier((contrib[:band], contrib[band + spheres :]))
    from_next = passed_along(sends[0], CELLS, -1)
    from_prev = passed_along(sends[1], CELLS, 1)

    padded = jnp.concatenate([from_prev_rows, source, from_next_rows], axis=0)
    padded, blocks_half, unused = lax.optimization_barrier((padded, blocks_half, contrib))
    gathered = jnp.einsum(
        "kse,ex->ksx", blocks_half, padded, preferred_element_type=jnp.float32
    ).astype(jnp.bfloat16)
    coupled = jnp.einsum(
        "ksdc,kcf->sdf",
        gathered.reshape(classes, spheres, groups, order),
        translations,
        preferred_element_type=jnp.float32,
    ).reshape(spheres, columns)

    back = contrib[band : band + spheres]
    back = back.at[spheres - band :].add(from_next)
    back = back.at[:band].add(from_prev)

    scattered = gain * coupled
    image = incident - scattered
    dual_image = incident - back

    partial = jnp.sum(
        jnp.stack([incident * incident, incident * scattered, incident * back, scattered * back]), axis=1
    )
    partial = jnp.sum(lax.optimization_barrier(partial), axis=1)
    partial = lax.optimization_barrier(partial)
    total = exchange_sum(exchange_sum(partial, ("z", "core")), ("y", DIRS))
    rows = lax.optimization_barrier(jnp.broadcast_to(total[:, None], (4, columns)))
    norm_old = rows[0:1]
    cross_u = rows[1:2]
    cross_v = rows[2:3]
    cross_uv = rows[3:4]
    curvature = norm_old - cross_u
    step_size = norm_old / curvature
    keep = -cross_u / curvature
    norm_new = keep * keep * norm_old + keep * step_size * (cross_u + cross_v) + step_size * step_size * cross_uv

    solution = step_size * incident
    residual = incident - step_size * image
    dual_residual = incident - step_size * dual_image
    direction = residual + norm_new / norm_old * incident
    return (solution, residual, dual_residual, direction)


def physical_mesh(mesh):
    devices = mesh.devices
    cores = len({d.core_on_chip for d in devices.flat})
    rows = len({d.coords[1] for d in devices.flat})
    depth = devices.shape[0] // (rows * cores)
    return Mesh(devices.reshape(rows, depth, cores, devices.shape[1]), CELLS + (DIRS,))


def solution(mesh):
    placed = (
        P(CELLS, DIRS),
        P(CELLS, None),
        P(),
        P(CELLS, None),
        P(CELLS, None),
        P(CELLS, None),
        P(CELLS, None),
    )
    return jax.shard_map(
        on_device,
        mesh=physical_mesh(mesh),
        in_specs=placed,
        out_specs=(P(CELLS, DIRS), P(CELLS, DIRS), P(CELLS, DIRS), P(CELLS, DIRS)),
        check_vma=False,
    )
```

```python
import jax
import jax.numpy as jnp
from jax import lax
from jax.sharding import Mesh, PartitionSpec as P


def passed_along(x, axes, by):
    devices = 1
    for axis in axes:
        devices *= lax.axis_size(axis)
    return lax.ppermute(x, axes, [(i, (i + by) % devices) for i in range(devices)])


CELLS = ("y", "z", "core")
DIRS = "x"


def exchange_sum(v, axes):
    members = 1
    for axis in axes:
        members *= lax.axis_size(axis)
    spread = jnp.broadcast_to(v[None, :], (members,) + v.shape)
    return jnp.sum(lax.all_to_all(spread, axes, 0, 0, tiled=True), axis=0)


def on_device(incident, scattering, translations, pair_sphere, pair_class, pair_weight, pair_mask):
    spheres = incident.shape[0]
    columns = incident.shape[1]
    order = translations.shape[1]
    groups = columns // order
    classes = translations.shape[0]
    slots = pair_sphere.shape[1]
    band = spheres // 2
    extent = spheres + 2 * band
    position = lax.axis_index(CELLS)
    cell_count = lax.axis_size("y") * lax.axis_size("z") * lax.axis_size("core")

    source = incident.astype(jnp.bfloat16)
    last_rows, first_rows, scattering = lax.optimization_barrier(
        (incident[spheres - band :].astype(jnp.bfloat16), incident[:band].astype(jnp.bfloat16), scattering)
    )
    from_prev_rows = passed_along(last_rows, CELLS, 1)
    from_next_rows = passed_along(first_rows, CELLS, -1)

    owner = pair_sphere // spheres
    within = pair_sphere % spheres
    offset = (owner - position) % cell_count
    column = jnp.where(
        offset == 0,
        band + within,
        jnp.where(offset == 1, band + spheres + within, within - (spheres - band)),
    )
    placed = (column[:, :, None] == jnp.arange(extent, dtype=jnp.int32)[None, None, :]).astype(
        jnp.bfloat16
    )
    strength = pair_weight.astype(jnp.float32) * pair_mask.astype(jnp.float32)
    chosen = pair_class[:, :, None] == jnp.arange(classes, dtype=jnp.int32)[None, None, :]
    coupling = jnp.where(chosen, strength[:, :, None], jnp.float32(0.0)).astype(jnp.bfloat16)
    blocks = jnp.einsum("smk,sme->kse", coupling, placed, preferred_element_type=jnp.float32)
    blocks_half = blocks.astype(jnp.bfloat16)

    gain = jnp.tile(scattering, (1, groups))
    weighted = (gain * incident).astype(jnp.bfloat16).reshape(spheres, groups, order)
    moved = jnp.einsum(
        "sdc,kfc->ksdf", weighted, translations, preferred_element_type=jnp.float32
    ).reshape(classes, spheres, columns)
    contrib = jnp.einsum(
        "kse,ksx->ex",
        blocks,
        moved,
        precision=lax.Precision.HIGH,
        preferred_element_type=jnp.float32,
    )
    sends = lax.optimization_barrier((contrib[:band], contrib[band + spheres :]))
    from_next = passed_along(sends[0], CELLS, -1)
    from_prev = passed_along(sends[1], CELLS, 1)

    padded = jnp.concatenate([from_prev_rows, source, from_next_rows], axis=0)
    padded, blocks_half, unused = lax.optimization_barrier((padded, blocks_half, contrib))
    gathered = jnp.einsum(
        "kse,ex->ksx", blocks_half, padded, preferred_element_type=jnp.float32
    ).astype(jnp.bfloat16)
    coupled = jnp.einsum(
        "ksdc,kcf->sdf",
        gathered.reshape(classes, spheres, groups, order),
        translations,
        preferred_element_type=jnp.float32,
    ).reshape(spheres, columns)

    back = contrib[band : band + spheres]
    back = back.at[spheres - band :].add(from_next)
    back = back.at[:band].add(from_prev)

    scattered = gain * coupled
    image = incident - scattered
    dual_image = incident - back

    partial = jnp.sum(
        jnp.stack([incident * incident, incident * scattered, incident * back, scattered * back]), axis=1
    )
    partial = jnp.sum(lax.optimization_barrier(partial), axis=1)
    partial = lax.optimization_barrier(partial)
    total = exchange_sum(exchange_sum(partial, ("z", "core")), ("y", DIRS))
    rows = lax.optimization_barrier(jnp.broadcast_to(total[:, None], (4, columns)))
    norm_old = rows[0:1]
    cross_u = rows[1:2]
    cross_v = rows[2:3]
    cross_uv = rows[3:4]
    curvature = norm_old - cross_u
    step_size = norm_old / curvature
    keep = -cross_u / curvature
    norm_new = keep * keep * norm_old + keep * step_size * (cross_u + cross_v) + step_size * step_size * cross_uv

    solution = step_size * incident
    residual = incident - step_size * image
    dual_residual = incident - step_size * dual_image
    direction = residual + norm_new / norm_old * incident
    return (solution, residual, dual_residual, direction)


def physical_mesh(mesh):
    devices = mesh.devices
    cores = len({d.core_on_chip for d in devices.flat})
    rows = len({d.coords[1] for d in devices.flat})
    depth = devices.shape[0] // (rows * cores)
    return Mesh(devices.reshape(rows, depth, cores, devices.shape[1]), CELLS + (DIRS,))


def solution(mesh):
    placed = (
        P(CELLS, DIRS),
        P(CELLS, None),
        P(),
        P(CELLS, None),
        P(CELLS, None),
        P(CELLS, None),
        P(CELLS, None),
    )
    return jax.shard_map(
        on_device,
        mesh=physical_mesh(mesh),
        in_specs=placed,
        out_specs=(P(CELLS, DIRS), P(CELLS, DIRS), P(CELLS, DIRS), P(CELLS, DIRS)),
        check_vma=False,
    )
```
